1024 devices in a mesh: expert: 64 (over z, core), mp: 16 (over y, x).
Axes of the slice: x: 4, y: 4, z: 32, core: 2. Of those that a mesh axis runs over, the one named last changes fastest.
Arguments:
- tokens: bfloat16 [8192, 4096], P('expert', 'mp'), may hold values from -6 to 6
- expert_ids: int32 [8192, 1], P('expert'), may hold values from 0 to 63; in each aligned block of 128 rows (0 to 127, 128 to 255, ...) at most 4 rows name the same one
- seq_lengths: int32 [64], P('expert'), may hold values from 64 to 128, as said below
- hidden_cotangent: bfloat16 [64, 256, 6144], P('expert', None, 'mp'), may hold values from -6 to 6
- w_in: bfloat16 [64, 4096, 6144], P('expert', None, 'mp'), may hold values from -0.09375 to 0.09375
Outputs:
- grad_tokens: bfloat16 [8192, 4096], P('expert', 'mp')
The draws below stay inside these ranges and needn't reach their ends.
Inputs may be any that keep to these rules, and one draw needn't show every extreme that they name: `expert_ids`: in each aligned block of 128 rows no expert is named by more than 4 rows, a bound that some block reaches. `seq_lengths`: some sequence is full and some has exactly 64 live positions.
All inputs are finite; a program needn't handle non-finite values.
Results may differ from the reference program's by a relative error of at most 0.014.
Values may be sent and summed in bfloat16 or wider, within the bound.
No kernel may reach another device: no remote copies, remote signals or barrier semaphores. Data moves between devices by JAX's collectives and lax.ppermute only.
A program may use at most 32 MiB of HBM per device.

```python
import math
import jax
import jax.numpy as jnp
import numpy as np
from jax import lax

D = 4096
FF = 6144
SEQ_LEN = 128
TOK_DEV = 128
EXPERTS = 64
CAP = 4
SLOTS = 256
TOKENS = 8192
SEQS = 64
N_EXPERT = 64
N_MP = 16


def draw_seq_lengths(key, part):
    key_one, key_two, key_three = jax.random.split(jax.random.fold_in(key, 17), 3)
    lengths = jax.random.randint(key_one, (SEQS,), SEQ_LEN // 2, SEQ_LEN + 1)
    first = jax.random.randint(key_two, (), 0, SEQS)
    second = (first + 1 + jax.random.randint(key_three, (), 0, SEQS - 1)) % SEQS
    lengths = lengths.at[first].set(SEQ_LEN).at[second].set(SEQ_LEN // 2)
    return lengths.astype(jnp.int32)


def block_scale(rng, shape, shards, smallest, largest):
    def one(dim, blocks):
        steps = jax.random.uniform(jax.random.fold_in(jax.random.fold_in(rng, 6), dim), (blocks,), jnp.float32, smallest / len(shards), largest / len(shards))
        return jnp.repeat(jnp.exp(steps), shape[dim] // blocks).reshape((-1,) + (1,) * (len(shape) - dim - 1))

    loudness = one(*shards[0])
    for cut in shards[1:]:
        loudness = loudness * one(*cut)
    return loudness


def shared_out(rng, own, number, rows, count, top, bound, skew):
    order = jax.random.permutation(rng, count)
    crowded, usual = load_shares(count, rows * top, bound, skew, True), load_shares(count, rows * top, bound, skew, False)
    places = jnp.arange(count)

    def named(tallies, offset_by):
        used = int((tallies > 0).sum())
        fixed = max(1, used // 4)
        moved = fixed + (places - fixed + offset_by * (used - fixed)) % max(1, count - fixed)
        return jnp.zeros((count,), jnp.int32).at[order[jnp.where(places < fixed, places, moved)]].set(jnp.asarray(tallies, jnp.int32))

    tallies = jnp.where(number % 4 == 0, named(crowded, number // 4), named(usual, number - number // 4 - 1))
    mixed = jax.random.permutation(jax.random.fold_in(own, 3), count)
    giver, sink = mixed[0:count // 2 * 2:2], mixed[1:count // 2 * 2:2]
    room = jnp.minimum(tallies[giver] - 1, bound - tallies[sink]) // 2
    room = jnp.where((giver == order[0]) | (sink == order[0]) | (tallies[sink] == 0), 0, jnp.maximum(room, 0))
    moved = jax.random.randint(jax.random.fold_in(own, 4), (count // 2,), 0, 1 << 20) % (room + 1)
    tallies = tallies.at[giver].add(-moved).at[sink].add(moved)
    labels = jnp.searchsorted(jnp.cumsum(tallies), jnp.arange(rows * top), side="right").astype(jnp.int32)
    grid = labels.reshape(top, rows).T
    grid = grid[jax.random.permutation(jax.random.fold_in(own, 1), rows)]
    offset_by = jax.random.randint(jax.random.fold_in(own, 2), (rows, 1), 0, top)
    return jnp.take_along_axis(grid, (jnp.arange(top)[None, :] + offset_by) % top, axis=1)


def load_shares(amount, total, most, slope, full):
    loads = [(1 << 20) // math.isqrt(rank ** slope) + 1 for rank in range(1, amount + 1)]
    largest = most if full else min(most, max(-(-total // amount), total * loads[0] // sum(loads)))
    least = 1 if total - largest >= amount - 1 else 0
    counts, spare = [largest] + [least] * (amount - 1), total - largest - least * (amount - 1)
    while spare > 0:
        candidates = [i for i in range(1, amount) if counts[i] < largest] or [i for i in range(1, amount) if counts[i] < most]
        pool, budget = sum([loads[i] for i in candidates]), spare
        for i in candidates:
            extra = min(most - counts[i], max(1, budget * loads[i] // pool), spare)
            counts[i] = counts[i] + extra
            spare = spare - extra
    return np.array(counts)


def scatter_about(rng, extent, spread, bound, cuts=(), kind=jnp.bfloat16):
    array = jax.random.normal(rng, extent, jnp.float32) * spread
    if len(cuts) > 0:
        array = block_scale(rng, extent, cuts, -0.22, 0.18) * array
    return jnp.clip(array, min=-bound, max=bound).astype(kind)


def setup_inputs(seed: int = 0) -> dict:
    key_list = jax.random.split(jax.random.key(seed), 6)
    tokens = scatter_about(key_list[0], (TOKENS, D), 1.0, 6.0, ((0, 64), (1, 16)))
    expert_ids_keys = jax.random.split(jax.random.fold_in(key_list[1], 1), TOKENS // TOK_DEV)
    expert_ids_turns = jax.random.permutation(jax.random.fold_in(key_list[1], 3), TOKENS // TOK_DEV)
    expert_ids = jax.vmap(lambda own, number: shared_out(jax.random.fold_in(key_list[1], 2), own, number, TOK_DEV, EXPERTS, 1, CAP, 2))(expert_ids_keys, expert_ids_turns).reshape((TOKENS, 1))
    seq_lengths = draw_seq_lengths(jax.random.fold_in(key_list[5], 71), 0)
    hidden_cotangent = scatter_about(key_list[3], (EXPERTS, SLOTS, FF), 1.0, 6.0, ((0, 64), (2, 16)))
    w_in = scatter_about(key_list[4], (EXPERTS, D, FF), D ** -0.5, 0.09375, ((0, 64), (2, 16)))
    return {"tokens": tokens, "expert_ids": expert_ids, "seq_lengths": seq_lengths, "hidden_cotangent": hidden_cotangent, "w_in": w_in}


def gelu_slope(preact):
    coeff = math.sqrt(2.0 / math.pi)
    squashed = jnp.tanh(coeff * (preact + 0.044715 * preact * preact * preact))
    return 0.5 * (1.0 + squashed) + 0.5 * preact * (1.0 - squashed * squashed) * coeff * (1.0 + 3.0 * 0.044715 * preact * preact)

def reference(tokens, expert_ids, seq_lengths, hidden_cotangent, w_in):
    slot_count = N_EXPERT * CAP
    position = jnp.arange(TOKENS, dtype=jnp.int32)
    seq_length = seq_lengths[position // SEQ_LEN]
    live_mask = (position % SEQ_LEN < seq_length).reshape(N_EXPERT, TOK_DEV)
    expert_row = expert_ids[:, 0].reshape(N_EXPERT, TOK_DEV)
    onehot = ((expert_row[:, :, None] == jnp.arange(EXPERTS, dtype=jnp.int32)[None, None, :]) & live_mask[:, :, None]).astype(jnp.int32)
    slot_rank = lax.optimization_barrier(jnp.sum(jnp.cumsum(onehot, axis=1) * onehot, axis=2)) - 1
    source = jnp.arange(N_EXPERT, dtype=jnp.int32)[:, None]
    target = jnp.where(live_mask, expert_row * slot_count + source * CAP + slot_rank, EXPERTS * slot_count).reshape(-1).astype(jnp.int32)
    buffer = jnp.zeros((EXPERTS * slot_count + 1, D), tokens.dtype).at[target].set(tokens)
    slot_tokens = buffer[:-1].reshape(EXPERTS, slot_count, D)

    def per_expert(inputs):
        features, cotangent, weight = inputs
        pre_act = jnp.dot(features, weight, preferred_element_type=jnp.float32)
        hidden_grad = (cotangent.astype(jnp.float32) * gelu_slope(pre_act)).astype(jnp.bfloat16)
        blocks = hidden_grad.reshape(slot_count, N_MP, FF // N_MP).astype(jnp.float32)
        weight_blocks = weight.reshape(D, N_MP, FF // N_MP).astype(jnp.float32)
        block_parts = jnp.einsum('rmf,dmf->mrd', blocks, weight_blocks).astype(jnp.bfloat16)
        block_parts = lax.optimization_barrier(block_parts)
        return lax.optimization_barrier(jnp.sum(block_parts.astype(jnp.float32), axis=0)).astype(jnp.bfloat16)
    slot_grads = lax.map(per_expert, (slot_tokens, hidden_cotangent, w_in))
    flat_grads = jnp.concatenate([slot_grads.reshape(EXPERTS * slot_count, D), jnp.zeros((1, D), jnp.bfloat16)], axis=0)
    return flat_grads[target]
```

```python
import math

import jax
import jax.numpy as jnp
from jax import lax
from jax.sharding import PartitionSpec as P

SEQ_LEN = 128


def gelu_slope(preact):
    coeff = math.sqrt(2.0 / math.pi)
    squashed = jnp.tanh(coeff * (preact + 0.044715 * preact * preact * preact))
    return 0.5 * (1.0 + squashed) + 0.5 * preact * (1.0 - squashed * squashed) * coeff * (
        1.0 + 3.0 * 0.044715 * preact * preact
    )


def mp_grid():
    n_mp = lax.axis_size("mp")
    nx = math.isqrt(n_mp)
    return n_mp, nx, n_mp // nx


def shift_x(shift):
    n_mp, nx, ny = mp_grid()
    return [(y * nx + x, y * nx + (x + shift) % nx) for y in range(ny) for x in range(nx)]


def shift_y(shift):
    n_mp, nx, ny = mp_grid()
    return [(y * nx + x, ((y + shift) % ny) * nx + x) for y in range(ny) for x in range(nx)]


def gather_mp(block):
    n_mp, nx, ny = mp_grid()
    me = lax.axis_index("mp")
    my_y, my_x = me // nx, me % nx
    with jax.named_scope("gather_along_x"):
        pieces = [block] + [lax.ppermute(block, "mp", shift_x(s)) for s in range(1, nx)]
        along_x = jnp.take(jnp.stack(pieces), (my_x - jnp.arange(nx)) % nx, axis=0)
    with jax.named_scope("gather_along_y"):
        pieces = [along_x] + [lax.ppermute(along_x, "mp", shift_y(s)) for s in range(1, ny)]
        full = jnp.take(jnp.stack(pieces), (my_y - jnp.arange(ny)) % ny, axis=0)
    return full.reshape((n_mp,) + block.shape)


def reduce_scatter_mp(parts):
    n_mp, nx, ny = mp_grid()
    me = lax.axis_index("mp")
    my_y, my_x = me // nx, me % nx
    grouped = parts.reshape((ny, nx) + parts.shape[1:])
    with jax.named_scope("reduce_along_y"):
        acc = lax.dynamic_index_in_dim(grouped, my_y, 0, keepdims=False).astype(jnp.float32)
        for s in range(1, ny):
            send = lax.dynamic_index_in_dim(grouped, (my_y + s) % ny, 0, keepdims=False)
            acc = acc + lax.ppermute(send, "mp", shift_y(s)).astype(jnp.float32)
    with jax.named_scope("reduce_along_x"):
        total = lax.dynamic_index_in_dim(acc, my_x, 0, keepdims=False)
        for s in range(1, nx):
            send = lax.dynamic_index_in_dim(acc, (my_x + s) % nx, 0, keepdims=False)
            total = total + lax.ppermute(send, "mp", shift_x(s))
    return total


def per_device(tokens, expert_ids, seq_lengths, hidden_cotangent, w_in):
    tok_dev = tokens.shape[0]
    experts = w_in.shape[0] * lax.axis_size("expert")
    capacity = max(2, 2 * tok_dev // experts)
    position = jnp.arange(tok_dev, dtype=jnp.int32)
    seq_index = position // SEQ_LEN
    seq_length = jnp.sum(
        jnp.where(
            seq_index[:, None] == jnp.arange(seq_lengths.shape[0], dtype=jnp.int32)[None, :],
            seq_lengths[None, :],
            0,
        ),
        axis=1,
    )
    live_mask = position % SEQ_LEN < seq_length
    expert_row = expert_ids[:, 0]
    onehot = (
        (expert_row[:, None] == jnp.arange(experts, dtype=jnp.int32)[None, :]) & live_mask[:, None]
    ).astype(jnp.int32)
    slot_rank = jnp.sum(jnp.cumsum(onehot, axis=0) * onehot, axis=1) - 1
    target = jnp.where(live_mask, expert_row * capacity + slot_rank, experts * capacity)
    buffer = (
        jnp.zeros((experts * capacity + 1,) + tokens.shape[1:], tokens.dtype).at[target].set(tokens)
    )
    arrived = lax.all_to_all(
        buffer[:-1].reshape((experts, capacity) + tokens.shape[1:]),
        "expert",
        split_axis=0,
        concat_axis=0,
        tiled=True,
    )
    slot_count = arrived.shape[0] * capacity
    n_mp = lax.axis_size("mp")
    blocks = gather_mp(arrived.reshape(slot_count, arrived.shape[2]))
    weight = w_in[0]
    weight_blocks = weight.reshape((n_mp, weight.shape[0] // n_mp, weight.shape[1]))
    pre_act = jnp.einsum(
        "jsk,jkf->sf", blocks, weight_blocks, preferred_element_type=jnp.float32
    )
    hidden_grad = (hidden_cotangent[0].astype(jnp.float32) * gelu_slope(pre_act)).astype(
        jnp.bfloat16
    )
    block_parts = jnp.einsum(
        "sf,jkf->jsk", hidden_grad, weight_blocks, preferred_element_type=jnp.float32
    ).astype(jnp.bfloat16)
    summed = reduce_scatter_mp(block_parts).astype(jnp.bfloat16)
    returned = lax.all_to_all(
        summed.reshape(arrived.shape[0], capacity, summed.shape[1]),
        "expert",
        split_axis=0,
        concat_axis=0,
        tiled=True,
    )
    flat_rows = returned.reshape((experts * capacity,) + returned.shape[2:])
    padded = jnp.concatenate(
        [flat_rows, jnp.zeros((1,) + flat_rows.shape[1:], flat_rows.dtype)], axis=0
    )
    return padded[target]


def solution(mesh):
    in_specs = (
        P("expert", "mp"),
        P("expert", None),
        P("expert"),
        P("expert", None, "mp"),
        P("expert", None, "mp"),
    )
    out_specs = P("expert", "mp")
    return jax.shard_map(
        per_device, mesh=mesh, in_specs=in_specs, out_specs=out_specs, check_vma=False
    )
```

```python
import math

import jax
import jax.numpy as jnp
from jax import lax
from jax.sharding import PartitionSpec as P

SEQ_LEN = 128


def gelu_slope(preact):
    coeff = math.sqrt(2.0 / math.pi)
    squashed = jnp.tanh(coeff * (preact + 0.044715 * preact * preact * preact))
    return 0.5 * (1.0 + squashed) + 0.5 * preact * (1.0 - squashed * squashed) * coeff * (
        1.0 + 3.0 * 0.044715 * preact * preact
    )


def gather_mp(block):
    n_mp = lax.axis_size("mp")
    copies = jnp.broadcast_to(block[None], (n_mp,) + block.shape)
    return lax.all_to_all(copies, "mp", split_axis=0, concat_axis=0, tiled=True)


def reduce_scatter_mp(parts):
    arrived = lax.all_to_all(parts, "mp", split_axis=0, concat_axis=0, tiled=True)
    return jnp.sum(arrived.astype(jnp.float32), axis=0)


def per_device(tokens, expert_ids, seq_lengths, hidden_cotangent, w_in):
    tok_dev = tokens.shape[0]
    experts = w_in.shape[0] * lax.axis_size("expert")
    capacity = max(2, 2 * tok_dev // experts)
    position = jnp.arange(tok_dev, dtype=jnp.int32)
    seq_index = position // SEQ_LEN
    seq_length = jnp.sum(
        jnp.where(
            seq_index[:, None] == jnp.arange(seq_lengths.shape[0], dtype=jnp.int32)[None, :],
            seq_lengths[None, :],
            0,
        ),
        axis=1,
    )
    live_mask = position % SEQ_LEN < seq_length
    expert_row = expert_ids[:, 0]
    onehot = (
        (expert_row[:, None] == jnp.arange(experts, dtype=jnp.int32)[None, :]) & live_mask[:, None]
    ).astype(jnp.int32)
    slot_rank = jnp.sum(jnp.cumsum(onehot, axis=0) * onehot, axis=1) - 1
    target = jnp.where(live_mask, expert_row * capacity + slot_rank, experts * capacity)
    buffer = (
        jnp.zeros((experts * capacity + 1,) + tokens.shape[1:], tokens.dtype).at[target].set(tokens)
    )
    arrived = lax.all_to_all(
        buffer[:-1].reshape((experts, capacity) + tokens.shape[1:]),
        "expert",
        split_axis=0,
        concat_axis=0,
        tiled=True,
    )
    slot_count = arrived.shape[0] * capacity
    n_mp = lax.axis_size("mp")
    blocks = gather_mp(arrived.reshape(slot_count, arrived.shape[2]))
    weight = w_in[0]
    weight_blocks = weight.reshape((n_mp, weight.shape[0] // n_mp, weight.shape[1]))
    pre_act = jnp.einsum(
        "jsk,jkf->sf", blocks, weight_blocks, preferred_element_type=jnp.float32
    )
    hidden_grad = (hidden_cotangent[0].astype(jnp.float32) * gelu_slope(pre_act)).astype(
        jnp.bfloat16
    )
    block_parts = jnp.einsum(
        "sf,jkf->jsk", hidden_grad, weight_blocks, preferred_element_type=jnp.float32
    ).astype(jnp.bfloat16)
    summed = reduce_scatter_mp(block_parts).astype(jnp.bfloat16)
    returned = lax.all_to_all(
        summed.reshape(arrived.shape[0], capacity, summed.shape[1]),
        "expert",
        split_axis=0,
        concat_axis=0,
        tiled=True,
    )
    flat_rows = returned.reshape((experts * capacity,) + returned.shape[2:])
    padded = jnp.concatenate(
        [flat_rows, jnp.zeros((1,) + flat_rows.shape[1:], flat_rows.dtype)], axis=0
    )
    return padded[target]


def solution(mesh):
    in_specs = (
        P("expert", "mp"),
        P("expert", None),
        P("expert"),
        P("expert", None, "mp"),
        P("expert", None, "mp"),
    )
    out_specs = P("expert", "mp")
    return jax.shard_map(
        per_device, mesh=mesh, in_specs=in_specs, out_specs=out_specs, check_vma=False
    )
```

```python
import math

import jax
import jax.numpy as jnp
from jax import lax
from jax.sharding import Mesh, PartitionSpec as P

SEQ_LEN = 128


def gelu_slope(preact):
    coeff = math.sqrt(2.0 / math.pi)
    squashed = jnp.tanh(coeff * (preact + 0.044715 * preact * preact * preact))
    return 0.5 * (1.0 + squashed) + 0.5 * preact * (1.0 - squashed * squashed) * coeff * (
        1.0 + 3.0 * 0.044715 * preact * preact
    )


def gather_mp(block):
    n_mp = lax.axis_size("mp")
    copies = jnp.broadcast_to(block[None], (n_mp,) + block.shape)
    return lax.all_to_all(copies, "mp", split_axis=0, concat_axis=0, tiled=True)


def reduce_scatter_mp(parts):
    arrived = lax.all_to_all(parts, "mp", split_axis=0, concat_axis=0, tiled=True)
    return jnp.sum(arrived.astype(jnp.float32), axis=0)


def exchange_experts(rows, back):
    n_ez, n_core = lax.axis_size("ez"), lax.axis_size("core")
    grid = rows.reshape((n_ez, n_core) + rows.shape[1:])
    if back:
        grid = lax.all_to_all(grid, "ez", split_axis=0, concat_axis=0, tiled=True)
        grid = lax.all_to_all(grid, "core", split_axis=1, concat_axis=1, tiled=True)
    else:
        grid = lax.all_to_all(grid, "core", split_axis=1, concat_axis=1, tiled=True)
        grid = lax.all_to_all(grid, "ez", split_axis=0, concat_axis=0, tiled=True)
    return grid.reshape(rows.shape)


def per_device(tokens, expert_ids, seq_lengths, hidden_cotangent, w_in):
    tok_dev = tokens.shape[0]
    n_ez, n_core = lax.axis_size("ez"), lax.axis_size("core")
    experts = w_in.shape[0] * n_ez * n_core
    capacity = max(2, 2 * tok_dev // experts)
    position = jnp.arange(tok_dev, dtype=jnp.int32)
    seq_index = position // SEQ_LEN
    seq_length = jnp.sum(
        jnp.where(
            seq_index[:, None] == jnp.arange(seq_lengths.shape[0], dtype=jnp.int32)[None, :],
            seq_lengths[None, :],
            0,
        ),
        axis=1,
    )
    live_mask = position % SEQ_LEN < seq_length
    expert_row = expert_ids[:, 0]
    onehot = (
        (expert_row[:, None] == jnp.arange(experts, dtype=jnp.int32)[None, :]) & live_mask[:, None]
    ).astype(jnp.int32)
    slot_rank = jnp.sum(jnp.cumsum(onehot, axis=0) * onehot, axis=1) - 1
    target = jnp.where(live_mask, expert_row * capacity + slot_rank, experts * capacity)
    buffer = (
        jnp.zeros((experts * capacity + 1,) + tokens.shape[1:], tokens.dtype).at[target].set(tokens)
    )
    arrived = exchange_experts(buffer[:-1].reshape((experts, capacity) + tokens.shape[1:]), False)
    slot_count = arrived.shape[0] * capacity
    n_mp = lax.axis_size("mp")
    blocks = gather_mp(arrived.reshape(slot_count, arrived.shape[2]))
    weight = w_in[0]
    weight_blocks = weight.reshape((n_mp, weight.shape[0] // n_mp, weight.shape[1]))
    pre_act = jnp.einsum(
        "jsk,jkf->sf", blocks, weight_blocks, preferred_element_type=jnp.float32
    )
    hidden_grad = (hidden_cotangent[0].astype(jnp.float32) * gelu_slope(pre_act)).astype(
        jnp.bfloat16
    )
    block_parts = jnp.einsum(
        "sf,jkf->jsk", hidden_grad, weight_blocks, preferred_element_type=jnp.float32
    ).astype(jnp.bfloat16)
    summed = reduce_scatter_mp(block_parts).astype(jnp.bfloat16)
    returned = exchange_experts(summed.reshape(arrived.shape[0], capacity, summed.shape[1]), True)
    flat_rows = returned.reshape((experts * capacity,) + returned.shape[2:])
    padded = jnp.concatenate(
        [flat_rows, jnp.zeros((1,) + flat_rows.shape[1:], flat_rows.dtype)], axis=0
    )
    return padded[target]


def solution(mesh):
    n_expert, n_mp = mesh.shape["expert"], mesh.shape["mp"]
    cores = 2
    split = Mesh(mesh.devices.reshape(n_expert // cores, cores, n_mp), ("ez", "core", "mp"))
    expert = ("ez", "core")
    in_specs = (
        P(expert, "mp"),
        P(expert, None),
        P(expert),
        P(expert, None, "mp"),
        P(expert, None, "mp"),
    )
    out_specs = P(expert, "mp")
    return jax.shard_map(
        per_device, mesh=split, in_specs=in_specs, out_specs=out_specs, check_vma=False
    )
```

```python
import math

import jax
import jax.numpy as jnp
from jax import lax
from jax.sharding import PartitionSpec as P

SEQ_LEN = 128


def gelu_slope(preact):
    coeff = math.sqrt(2.0 / math.pi)
    squashed = jnp.tanh(coeff * (preact + 0.044715 * preact * preact * preact))
    return 0.5 * (1.0 + squashed) + 0.5 * preact * (1.0 - squashed * squashed) * coeff * (
        1.0 + 3.0 * 0.044715 * preact * preact
    )


def gather_mp(block):
    n_mp = lax.axis_size("mp")
    copies = jnp.broadcast_to(block[None], (n_mp,) + block.shape)
    return lax.all_to_all(copies, "mp", split_axis=0, concat_axis=0, tiled=True)


def reduce_scatter_mp(parts):
    arrived = lax.all_to_all(parts, "mp", split_axis=0, concat_axis=0, tiled=True)
    return jnp.sum(arrived.astype(jnp.float32), axis=0)


def per_device(tokens, expert_ids, seq_lengths, hidden_cotangent, w_in):
    tok_dev = tokens.shape[0]
    experts = w_in.shape[0] * lax.axis_size("expert")
    capacity = max(2, 2 * tok_dev // experts)
    position = jnp.arange(tok_dev, dtype=jnp.int32)
    seq_index = position // SEQ_LEN
    seq_length = jnp.sum(
        jnp.where(
            seq_index[:, None] == jnp.arange(seq_lengths.shape[0], dtype=jnp.int32)[None, :],
            seq_lengths[None, :],
            0,
        ),
        axis=1,
    )
    live_mask = position % SEQ_LEN < seq_length
    expert_row = expert_ids[:, 0]
    picks = (expert_row[:, None] == jnp.arange(experts, dtype=jnp.int32)[None, :]) & live_mask[:, None]
    picks = picks.astype(jnp.bfloat16)
    earlier = (position[None, :] < position[:, None]).astype(jnp.bfloat16)
    before = jnp.dot(earlier, picks, preferred_element_type=jnp.float32)
    slot_rank = jnp.sum(before * picks.astype(jnp.float32), axis=1).astype(jnp.int32)
    target = expert_row * capacity + slot_rank
    slot_ids = jnp.arange(experts * capacity, dtype=jnp.int32)
    slot_hot = ((target[:, None] == slot_ids[None, :]) & live_mask[:, None]).astype(tokens.dtype)
    buffer = lax.dot_general(
        slot_hot, tokens, (((0,), (0,)), ((), ())), preferred_element_type=jnp.float32
    ).astype(tokens.dtype)
    arrived = lax.all_to_all(
        buffer.reshape((experts, capacity) + tokens.shape[1:]),
        "expert",
        split_axis=0,
        concat_axis=0,
        tiled=True,
    )
    slot_count = arrived.shape[0] * capacity
    n_mp = lax.axis_size("mp")
    blocks = gather_mp(arrived.reshape(slot_count, arrived.shape[2]))
    weight = w_in[0]
    weight_blocks = weight.reshape((n_mp, weight.shape[0] // n_mp, weight.shape[1]))
    pre_act = jnp.einsum(
        "jsk,jkf->sf", blocks, weight_blocks, preferred_element_type=jnp.float32
    )
    hidden_grad = (hidden_cotangent[0].astype(jnp.float32) * gelu_slope(pre_act)).astype(
        jnp.bfloat16
    )
    block_parts = jnp.einsum(
        "sf,jkf->jsk", hidden_grad, weight_blocks, preferred_element_type=jnp.float32
    ).astype(jnp.bfloat16)
    summed = reduce_scatter_mp(block_parts).astype(jnp.bfloat16)
    returned = lax.all_to_all(
        summed.reshape(arrived.shape[0], capacity, summed.shape[1]),
        "expert",
        split_axis=0,
        concat_axis=0,
        tiled=True,
    )
    flat_rows = returned.reshape((experts * capacity,) + returned.shape[2:])
    return jnp.dot(slot_hot, flat_rows, preferred_element_type=jnp.float32).astype(flat_rows.dtype)


def solution(mesh):
    in_specs = (
        P("expert", "mp"),
        P("expert", None),
        P("expert"),
        P("expert", None, "mp"),
        P("expert", None, "mp"),
    )
    out_specs = P("expert", "mp")
    return jax.shard_map(
        per_device, mesh=mesh, in_specs=in_specs, out_specs=out_specs, check_vma=False
    )
```

```python
import math

import jax
import jax.numpy as jnp
from jax import lax
from jax.experimental import pallas as pl
from jax.experimental.pallas import tpu as pltpu
from jax.sharding import PartitionSpec as P

SEQ_LEN = 128


def gelu_slope(preact):
    coeff = math.sqrt(2.0 / math.pi)
    squashed = jnp.tanh(coeff * (preact + 0.044715 * preact * preact * preact))
    return 0.5 * (1.0 + squashed) + 0.5 * preact * (1.0 - squashed * squashed) * coeff * (
        1.0 + 3.0 * 0.044715 * preact * preact
    )


def gather_mp(block):
    n_mp = lax.axis_size("mp")
    copies = jnp.broadcast_to(block[None], (n_mp,) + block.shape)
    return lax.all_to_all(copies, "mp", split_axis=0, concat_axis=0, tiled=True)


def hidden_kernel(features_ref, weight_ref, cotangent_ref, out_ref):
    n_blk, _, d_blk = features_ref.shape
    pre_act = jnp.zeros((features_ref.shape[1], weight_ref.shape[1]), jnp.float32)
    for j in range(n_blk):
        pre_act = pre_act + jnp.dot(
            features_ref[j], weight_ref[j * d_blk:(j + 1) * d_blk, :],
            preferred_element_type=jnp.float32,
        )
    hidden_grad = (cotangent_ref[...].astype(jnp.float32) * gelu_slope(pre_act)).astype(
        jnp.bfloat16
    )
    for j in range(n_blk):
        out_ref[j] = lax.dot_general(
            hidden_grad, weight_ref[j * d_blk:(j + 1) * d_blk, :],
            (((1,), (1,)), ((), ())), preferred_element_type=jnp.float32,
        ).astype(out_ref.dtype)


def block_parts_of(features, weight, cotangent):
    n_blk, slots, d_blk = features.shape
    ff = weight.shape[1]
    vmem = pl.BlockSpec(memory_space=pltpu.VMEM)
    return pl.pallas_call(
        hidden_kernel,
        out_shape=jax.ShapeDtypeStruct((n_blk, slots, d_blk), jnp.bfloat16),
        in_specs=[vmem, vmem, vmem],
        out_specs=vmem,
        cost_estimate=pl.CostEstimate(
            flops=4 * slots * n_blk * d_blk * ff,
            transcendentals=slots * ff,
            bytes_accessed=2 * (2 * features.size + weight.size + cotangent.size),
        ),
    )(features, weight, cotangent)


def sum_kernel(parts_ref, out_ref):
    total = parts_ref[0].astype(jnp.float32)
    for j in range(1, parts_ref.shape[0]):
        total = total + parts_ref[j].astype(jnp.float32)
    out_ref[...] = total.astype(out_ref.dtype)


def sum_blocks(parts):
    vmem = pl.BlockSpec(memory_space=pltpu.VMEM)
    return pl.pallas_call(
        sum_kernel,
        out_shape=jax.ShapeDtypeStruct(parts.shape[1:], jnp.bfloat16),
        in_specs=[vmem],
        out_specs=vmem,
        cost_estimate=pl.CostEstimate(
            flops=parts.size, transcendentals=0, bytes_accessed=2 * parts.size + parts.size // 8
        ),
    )(parts)


def reduce_scatter_mp(parts):
    arrived = lax.all_to_all(parts, "mp", split_axis=0, concat_axis=0, tiled=True)
    return sum_blocks(arrived)


def per_device(tokens, expert_ids, seq_lengths, hidden_cotangent, w_in):
    tok_dev = tokens.shape[0]
    experts = w_in.shape[0] * lax.axis_size("expert")
    capacity = max(2, 2 * tok_dev // experts)
    position = jnp.arange(tok_dev, dtype=jnp.int32)
    seq_index = position // SEQ_LEN
    seq_length = jnp.sum(
        jnp.where(
            seq_index[:, None] == jnp.arange(seq_lengths.shape[0], dtype=jnp.int32)[None, :],
            seq_lengths[None, :],
            0,
        ),
        axis=1,
    )
    live_mask = position % SEQ_LEN < seq_length
    expert_row = expert_ids[:, 0]
    picks = (expert_row[:, None] == jnp.arange(experts, dtype=jnp.int32)[None, :]) & live_mask[:, None]
    picks = picks.astype(jnp.bfloat16)
    earlier = (position[None, :] < position[:, None]).astype(jnp.bfloat16)
    before = jnp.dot(earlier, picks, preferred_element_type=jnp.float32)
    slot_rank = jnp.sum(before * picks.astype(jnp.float32), axis=1).astype(jnp.int32)
    target = expert_row * capacity + slot_rank
    slot_ids = jnp.arange(experts * capacity, dtype=jnp.int32)
    slot_hot = ((target[:, None] == slot_ids[None, :]) & live_mask[:, None]).astype(tokens.dtype)
    buffer = lax.dot_general(
        slot_hot, tokens, (((0,), (0,)), ((), ())), preferred_element_type=jnp.float32
    ).astype(tokens.dtype)
    arrived = lax.all_to_all(
        buffer.reshape((experts, capacity) + tokens.shape[1:]),
        "expert",
        split_axis=0,
        concat_axis=0,
        tiled=True,
    )
    slot_count = arrived.shape[0] * capacity
    n_mp = lax.axis_size("mp")
    blocks = gather_mp(arrived.reshape(slot_count, arrived.shape[2]))
    block_parts = block_parts_of(blocks, w_in[0], hidden_cotangent[0])
    summed = reduce_scatter_mp(block_parts).astype(jnp.bfloat16)
    returned = lax.all_to_all(
        summed.reshape(arrived.shape[0], capacity, summed.shape[1]),
        "expert",
        split_axis=0,
        concat_axis=0,
        tiled=True,
    )
    flat_rows = returned.reshape((experts * capacity,) + returned.shape[2:])
    return jnp.dot(slot_hot, flat_rows, preferred_element_type=jnp.float32).astype(flat_rows.dtype)


def solution(mesh):
    in_specs = (
        P("expert", "mp"),
        P("expert", None),
        P("expert"),
        P("expert", None, "mp"),
        P("expert", None, "mp"),
    )
    out_specs = P("expert", "mp")
    return jax.shard_map(
        per_device, mesh=mesh, in_specs=in_specs, out_specs=out_specs, check_vma=False
    )
```

```python
import math

import jax
import jax.numpy as jnp
from jax import lax
from jax.experimental import pallas as pl
from jax.experimental.pallas import tpu as pltpu
from jax.sharding import PartitionSpec as P

SEQ_LEN = 128


def gelu_slope(preact):
    coeff = math.sqrt(2.0 / math.pi)
    squashed = jnp.tanh(coeff * (preact + 0.044715 * preact * preact * preact))
    return 0.5 * (1.0 + squashed) + 0.5 * preact * (1.0 - squashed * squashed) * coeff * (
        1.0 + 3.0 * 0.044715 * preact * preact
    )


def gather_mp(block):
    n_mp = lax.axis_size("mp")
    copies = jnp.broadcast_to(block[None], (n_mp,) + block.shape)
    return lax.all_to_all(copies, "mp", split_axis=0, concat_axis=0, tiled=True)


def hidden_kernel(features_ref, weight_ref, cotangent_ref, out_ref, pre_ref, grad_ref, held_ref):
    phase, step = pl.program_id(0), pl.program_id(1)
    steps = pl.num_programs(1)
    per_step, _, d_blk = features_ref.shape
    rows = per_step * d_blk

    @pl.when(phase == 0)
    def _():
        @pl.when(step == 0)
        def _():
            pre_ref[...] = jnp.zeros_like(pre_ref)

        held_ref[pl.ds(pl.multiple_of(step * rows, rows), rows), :] = weight_ref[...]
        acc = pre_ref[...]
        for jj in range(per_step):
            acc = acc + jnp.dot(
                features_ref[jj], weight_ref[jj * d_blk:(jj + 1) * d_blk, :],
                preferred_element_type=jnp.float32,
            )
        pre_ref[...] = acc

        @pl.when(step == steps - 1)
        def _():
            grad_ref[...] = (
                cotangent_ref[...].astype(jnp.float32) * gelu_slope(pre_ref[...])
            ).astype(grad_ref.dtype)

    @pl.when(phase == 1)
    def _():
        hidden_grad = grad_ref[...]
        for jj in range(per_step):
            start = pl.multiple_of(step * rows + jj * d_blk, d_blk)
            out_ref[jj] = lax.dot_general(
                hidden_grad, held_ref[pl.ds(start, d_blk), :],
                (((1,), (1,)), ((), ())), preferred_element_type=jnp.float32,
            ).astype(out_ref.dtype)


def block_parts_of(features, weight, cotangent, steps=4):
    n_blk, slots, d_blk = features.shape
    d_model, ff = weight.shape
    per_step = n_blk // steps
    last = steps - 1
    return pl.pallas_call(
        hidden_kernel,
        out_shape=jax.ShapeDtypeStruct((n_blk, slots, d_blk), jnp.bfloat16),
        grid=(2, steps),
        in_specs=[
            pl.BlockSpec((per_step, slots, d_blk), lambda p, j: (j * (1 - p) + last * p, 0, 0)),
            pl.BlockSpec((per_step * d_blk, ff), lambda p, j: (j * (1 - p) + last * p, 0)),
            pl.BlockSpec((slots, ff), lambda p, j: (0, 0)),
        ],
        out_specs=pl.BlockSpec((per_step, slots, d_blk), lambda p, j: (j * p, 0, 0)),
        scratch_shapes=[
            pltpu.VMEM((slots, ff), jnp.float32),
            pltpu.VMEM((slots, ff), jnp.bfloat16),
            pltpu.VMEM((d_model, ff), jnp.bfloat16),
        ],
        compiler_params=pltpu.CompilerParams(dimension_semantics=("arbitrary", "arbitrary")),
        cost_estimate=pl.CostEstimate(
            flops=4 * slots * d_model * ff,
            transcendentals=slots * ff,
            bytes_accessed=2 * (2 * features.size + weight.size + cotangent.size),
        ),
    )(features, weight, cotangent)


def reduce_scatter_mp(parts):
    arrived = lax.all_to_all(parts, "mp", split_axis=0, concat_axis=0, tiled=True)
    return jnp.sum(arrived.astype(jnp.float32), axis=0)


def per_device(tokens, expert_ids, seq_lengths, hidden_cotangent, w_in):
    tok_dev = tokens.shape[0]
    experts = w_in.shape[0] * lax.axis_size("expert")
    capacity = max(2, 2 * tok_dev // experts)
    position = jnp.arange(tok_dev, dtype=jnp.int32)
    seq_index = position // SEQ_LEN
    seq_length = jnp.sum(
        jnp.where(
            seq_index[:, None] == jnp.arange(seq_lengths.shape[0], dtype=jnp.int32)[None, :],
            seq_lengths[None, :],
            0,
        ),
        axis=1,
    )
    live_mask = position % SEQ_LEN < seq_length
    expert_row = expert_ids[:, 0]
    picks = (expert_row[:, None] == jnp.arange(experts, dtype=jnp.int32)[None, :]) & live_mask[:, None]
    picks = picks.astype(jnp.bfloat16)
    earlier = (position[None, :] < position[:, None]).astype(jnp.bfloat16)
    before = jnp.dot(earlier, picks, preferred_element_type=jnp.float32)
    slot_rank = jnp.sum(before * picks.astype(jnp.float32), axis=1).astype(jnp.int32)
    target = expert_row * capacity + slot_rank
    slot_ids = jnp.arange(experts * capacity, dtype=jnp.int32)
    slot_hot = ((target[:, None] == slot_ids[None, :]) & live_mask[:, None]).astype(tokens.dtype)
    buffer = lax.dot_general(
        slot_hot, tokens, (((0,), (0,)), ((), ())), preferred_element_type=jnp.float32
    ).astype(tokens.dtype)
    arrived = lax.all_to_all(
        buffer.reshape((experts, capacity) + tokens.shape[1:]),
        "expert",
        split_axis=0,
        concat_axis=0,
        tiled=True,
    )
    slot_count = arrived.shape[0] * capacity
    n_mp = lax.axis_size("mp")
    blocks = gather_mp(arrived.reshape(slot_count, arrived.shape[2]))
    block_parts = block_parts_of(blocks, w_in[0], hidden_cotangent[0])
    summed = reduce_scatter_mp(block_parts).astype(jnp.bfloat16)
    returned = lax.all_to_all(
        summed.reshape(arrived.shape[0], capacity, summed.shape[1]),
        "expert",
        split_axis=0,
        concat_axis=0,
        tiled=True,
    )
    flat_rows = returned.reshape((experts * capacity,) + returned.shape[2:])
    return jnp.dot(slot_hot, flat_rows, preferred_element_type=jnp.float32).astype(flat_rows.dtype)


def solution(mesh):
    in_specs = (
        P("expert", "mp"),
        P("expert", None),
        P("expert"),
        P("expert", None, "mp"),
        P("expert", None, "mp"),
    )
    out_specs = P("expert", "mp")
    return jax.shard_map(
        per_device, mesh=mesh, in_specs=in_specs, out_specs=out_specs, check_vma=False
    )
```

```python
import math

import jax
import jax.numpy as jnp
from jax import lax
from jax.experimental import pallas as pl
from jax.experimental.pallas import tpu as pltpu
from jax.sharding import PartitionSpec as P

SEQ_LEN = 128


def gelu_slope(preact):
    coeff = math.sqrt(2.0 / math.pi)
    squashed = jnp.tanh(coeff * (preact + 0.044715 * preact * preact * preact))
    return 0.5 * (1.0 + squashed) + 0.5 * preact * (1.0 - squashed * squashed) * coeff * (
        1.0 + 3.0 * 0.044715 * preact * preact
    )


def gather_mp(block):
    n_mp = lax.axis_size("mp")
    copies = jnp.broadcast_to(block[None], (n_mp,) + block.shape)
    return lax.all_to_all(copies, "mp", split_axis=0, concat_axis=0, tiled=True)


def hidden_kernel(features_ref, weight_ref, cotangent_ref, out_ref, pre_ref, grad_ref, held_ref):
    phase, step = pl.program_id(0), pl.program_id(1)
    steps = pl.num_programs(1)
    per_step, _, d_blk = features_ref.shape
    rows = per_step * d_blk

    @pl.when(phase == 0)
    def _():
        @pl.when(step == 0)
        def _():
            pre_ref[...] = jnp.zeros_like(pre_ref)

        held_ref[pl.ds(pl.multiple_of(step * rows, rows), rows), :] = weight_ref[...]
        acc = pre_ref[...]
        for jj in range(per_step):
            acc = acc + jnp.dot(
                features_ref[jj], weight_ref[jj * d_blk:(jj + 1) * d_blk, :],
                preferred_element_type=jnp.float32,
            )
        pre_ref[...] = acc

        @pl.when(step == steps - 1)
        def _():
            grad_ref[...] = (
                cotangent_ref[...].astype(jnp.float32) * gelu_slope(pre_ref[...])
            ).astype(grad_ref.dtype)

    @pl.when(phase == 1)
    def _():
        hidden_grad = grad_ref[...]
        for jj in range(per_step):
            start = pl.multiple_of(step * rows + jj * d_blk, d_blk)
            out_ref[jj] = lax.dot_general(
                hidden_grad, held_ref[pl.ds(start, d_blk), :],
                (((1,), (1,)), ((), ())), preferred_element_type=jnp.float32,
            ).astype(out_ref.dtype)


def block_parts_of(features, weight, cotangent, steps=2):
    n_blk, slots, d_blk = features.shape
    d_model, ff = weight.shape
    per_step = n_blk // steps
    last = steps - 1
    return pl.pallas_call(
        hidden_kernel,
        out_shape=jax.ShapeDtypeStruct((n_blk, slots, d_blk), jnp.bfloat16),
        grid=(2, steps),
        in_specs=[
            pl.BlockSpec((per_step, slots, d_blk), lambda p, j: (j * (1 - p) + last * p, 0, 0)),
            pl.BlockSpec((per_step * d_blk, ff), lambda p, j: (j * (1 - p) + last * p, 0)),
            pl.BlockSpec((slots, ff), lambda p, j: (0, 0)),
        ],
        out_specs=pl.BlockSpec((per_step, slots, d_blk), lambda p, j: (j * p, 0, 0)),
        scratch_shapes=[
            pltpu.VMEM((slots, ff), jnp.float32),
            pltpu.VMEM((slots, ff), jnp.bfloat16),
            pltpu.VMEM((d_model, ff), jnp.bfloat16),
        ],
        compiler_params=pltpu.CompilerParams(dimension_semantics=("arbitrary", "arbitrary")),
        cost_estimate=pl.CostEstimate(
            flops=4 * slots * d_model * ff,
            transcendentals=slots * ff,
            bytes_accessed=2 * (2 * features.size + weight.size + cotangent.size),
        ),
    )(features, weight, cotangent)


def reduce_scatter_mp(parts):
    arrived = lax.all_to_all(parts, "mp", split_axis=0, concat_axis=0, tiled=True)
    return jnp.sum(arrived.astype(jnp.float32), axis=0)


def per_device(tokens, expert_ids, seq_lengths, hidden_cotangent, w_in):
    tok_dev = tokens.shape[0]
    experts = w_in.shape[0] * lax.axis_size("expert")
    capacity = max(2, 2 * tok_dev // experts)
    position = jnp.arange(tok_dev, dtype=jnp.int32)
    seq_index = position // SEQ_LEN
    seq_length = jnp.sum(
        jnp.where(
            seq_index[:, None] == jnp.arange(seq_lengths.shape[0], dtype=jnp.int32)[None, :],
            seq_lengths[None, :],
            0,
        ),
        axis=1,
    )
    live_mask = position % SEQ_LEN < seq_length
    expert_row = expert_ids[:, 0]
    picks = (expert_row[:, None] == jnp.arange(experts, dtype=jnp.int32)[None, :]) & live_mask[:, None]
    picks = picks.astype(jnp.bfloat16)
    earlier = (position[None, :] < position[:, None]).astype(jnp.bfloat16)
    before = jnp.dot(earlier, picks, preferred_element_type=jnp.float32)
    slot_rank = jnp.sum(before * picks.astype(jnp.float32), axis=1).astype(jnp.int32)
    target = expert_row * capacity + slot_rank
    slot_ids = jnp.arange(experts * capacity, dtype=jnp.int32)
    slot_hot = ((target[:, None] == slot_ids[None, :]) & live_mask[:, None]).astype(tokens.dtype)
    buffer = lax.dot_general(
        slot_hot, tokens, (((0,), (0,)), ((), ())), preferred_element_type=jnp.float32
    ).astype(tokens.dtype)
    arrived = lax.all_to_all(
        buffer.reshape((experts, capacity) + tokens.shape[1:]),
        "expert",
        split_axis=0,
        concat_axis=0,
        tiled=True,
    )
    slot_count = arrived.shape[0] * capacity
    n_mp = lax.axis_size("mp")
    blocks = gather_mp(arrived.reshape(slot_count, arrived.shape[2]))
    block_parts = block_parts_of(blocks, w_in[0], hidden_cotangent[0])
    summed = reduce_scatter_mp(block_parts).astype(jnp.bfloat16)
    returned = lax.all_to_all(
        summed.reshape(arrived.shape[0], capacity, summed.shape[1]),
        "expert",
        split_axis=0,
        concat_axis=0,
        tiled=True,
    )
    flat_rows = returned.reshape((experts * capacity,) + returned.shape[2:])
    return jnp.dot(slot_hot, flat_rows, preferred_element_type=jnp.float32).astype(flat_rows.dtype)


def solution(mesh):
    in_specs = (
        P("expert", "mp"),
        P("expert", None),
        P("expert"),
        P("expert", None, "mp"),
        P("expert", None, "mp"),
    )
    out_specs = P("expert", "mp")
    return jax.shard_map(
        per_device, mesh=mesh, in_specs=in_specs, out_specs=out_specs, check_vma=False
    )
```

```python
import math

import jax
import jax.numpy as jnp
from jax import lax
from jax.experimental import pallas as pl
from jax.experimental.pallas import tpu as pltpu
from jax.sharding import PartitionSpec as P

SEQ_LEN = 128


def gelu_slope(preact):
    coeff = math.sqrt(2.0 / math.pi)
    squashed = jnp.tanh(coeff * (preact + 0.044715 * preact * preact * preact))
    return 0.5 * (1.0 + squashed) + 0.5 * preact * (1.0 - squashed * squashed) * coeff * (
        1.0 + 3.0 * 0.044715 * preact * preact
    )


def gather_mp(block):
    n_mp = lax.axis_size("mp")
    copies = jnp.broadcast_to(block[None], (n_mp,) + block.shape)
    return lax.all_to_all(copies, "mp", split_axis=0, concat_axis=0, tiled=True)


def hidden_kernel(features_ref, weight_ref, cotangent_ref, out_ref, pre_ref, grad_ref, held_ref):
    phase, step = pl.program_id(0), pl.program_id(1)
    steps = pl.num_programs(1)
    per_step, _, d_blk = features_ref.shape
    rows = per_step * d_blk

    @pl.when(phase == 0)
    def _():
        @pl.when(step == 0)
        def _():
            pre_ref[...] = jnp.zeros_like(pre_ref)

        held_ref[pl.ds(pl.multiple_of(step * rows, rows), rows), :] = weight_ref[...]
        acc = pre_ref[...]
        for jj in range(per_step):
            acc = acc + jnp.dot(
                features_ref[jj], weight_ref[jj * d_blk:(jj + 1) * d_blk, :],
                preferred_element_type=jnp.float32,
            )
        pre_ref[...] = acc

        @pl.when(step == steps - 1)
        def _():
            grad_ref[...] = (
                cotangent_ref[...].astype(jnp.float32) * gelu_slope(pre_ref[...])
            ).astype(grad_ref.dtype)

    @pl.when(phase == 1)
    def _():
        hidden_grad = grad_ref[...]
        for jj in range(per_step):
            start = pl.multiple_of(step * rows + jj * d_blk, d_blk)
            out_ref[jj] = lax.dot_general(
                hidden_grad, held_ref[pl.ds(start, d_blk), :],
                (((1,), (1,)), ((), ())), preferred_element_type=jnp.float32,
            ).astype(out_ref.dtype)


def block_parts_of(features, weight, cotangent, steps=2):
    n_blk, slots, d_blk = features.shape
    d_model, ff = weight.shape
    per_step = n_blk // steps
    last = steps - 1
    return pl.pallas_call(
        hidden_kernel,
        out_shape=jax.ShapeDtypeStruct((n_blk, slots, d_blk), jnp.bfloat16),
        grid=(2, steps),
        in_specs=[
            pl.BlockSpec((per_step, slots, d_blk), lambda p, j: (j * (1 - p) + last * p, 0, 0)),
            pl.BlockSpec((per_step * d_blk, ff), lambda p, j: (j * (1 - p) + last * p, 0)),
            pl.BlockSpec((slots, ff), lambda p, j: (0, 0)),
        ],
        out_specs=pl.BlockSpec((per_step, slots, d_blk), lambda p, j: (j * p, 0, 0)),
        scratch_shapes=[
            pltpu.VMEM((slots, ff), jnp.float32),
            pltpu.VMEM((slots, ff), jnp.bfloat16),
            pltpu.VMEM((d_model, ff), jnp.bfloat16),
        ],
        compiler_params=pltpu.CompilerParams(dimension_semantics=("arbitrary", "arbitrary")),
        cost_estimate=pl.CostEstimate(
            flops=4 * slots * d_model * ff,
            transcendentals=slots * ff,
            bytes_accessed=2 * (2 * features.size + weight.size + cotangent.size),
        ),
    )(features, weight, cotangent)


def reduce_scatter_mp(parts):
    arrived = lax.all_to_all(parts, "mp", split_axis=0, concat_axis=0, tiled=True)
    return jnp.sum(arrived.astype(jnp.float32), axis=0)


def per_device(tokens, expert_ids, seq_lengths, hidden_cotangent, w_in):
    tok_dev = tokens.shape[0]
    experts = w_in.shape[0] * lax.axis_size("expert")
    capacity = max(2, 2 * tok_dev // experts)
    position = jnp.arange(tok_dev, dtype=jnp.int32)
    seq_index = position // SEQ_LEN
    seq_length = jnp.sum(
        jnp.where(
            seq_index[:, None] == jnp.arange(seq_lengths.shape[0], dtype=jnp.int32)[None, :],
            seq_lengths[None, :],
            0,
        ),
        axis=1,
    )
    live_mask = position % SEQ_LEN < seq_length
    expert_row = expert_ids[:, 0]
    same_before = (
        (expert_row[None, :] == expert_row[:, None])
        & live_mask[None, :]
        & (position[None, :] < position[:, None])
    )
    slot_rank = jnp.sum(same_before.astype(jnp.int32), axis=1)
    target = expert_row * capacity + slot_rank
    slot_ids = jnp.arange(experts * capacity, dtype=jnp.int32)
    slot_hot = ((target[:, None] == slot_ids[None, :]) & live_mask[:, None]).astype(tokens.dtype)
    buffer = lax.dot_general(
        slot_hot, tokens, (((0,), (0,)), ((), ())), preferred_element_type=jnp.float32
    ).astype(tokens.dtype)
    arrived = lax.all_to_all(
        buffer.reshape((experts, capacity) + tokens.shape[1:]),
        "expert",
        split_axis=0,
        concat_axis=0,
        tiled=True,
    )
    slot_count = arrived.shape[0] * capacity
    n_mp = lax.axis_size("mp")
    blocks = gather_mp(arrived.reshape(slot_count, arrived.shape[2]))
    block_parts = block_parts_of(blocks, w_in[0], hidden_cotangent[0])
    summed = reduce_scatter_mp(block_parts).astype(jnp.bfloat16)
    returned = lax.all_to_all(
        summed.reshape(arrived.shape[0], capacity, summed.shape[1]),
        "expert",
        split_axis=0,
        concat_axis=0,
        tiled=True,
    )
    flat_rows = returned.reshape((experts * capacity,) + returned.shape[2:])
    return jnp.dot(slot_hot, flat_rows, preferred_element_type=jnp.float32).astype(flat_rows.dtype)


def solution(mesh):
    in_specs = (
        P("expert", "mp"),
        P("expert", None),
        P("expert"),
        P("expert", None, "mp"),
        P("expert", None, "mp"),
    )
    out_specs = P("expert", "mp")
    return jax.shard_map(
        per_device, mesh=mesh, in_specs=in_specs, out_specs=out_specs, check_vma=False
    )
```

```python
import math

import jax
import jax.numpy as jnp
from jax import lax
from jax.experimental import pallas as pl
from jax.experimental.pallas import tpu as pltpu
from jax.sharding import PartitionSpec as P

SEQ_LEN = 128


def gelu_slope(preact):
    coeff = math.sqrt(2.0 / math.pi)
    squashed = jnp.tanh(coeff * (preact + 0.044715 * preact * preact * preact))
    return 0.5 * (1.0 + squashed) + 0.5 * preact * (1.0 - squashed * squashed) * coeff * (
        1.0 + 3.0 * 0.044715 * preact * preact
    )


def gather_mp(block):
    n_mp = lax.axis_size("mp")
    copies = jnp.broadcast_to(block[None], (n_mp,) + block.shape)
    return lax.all_to_all(copies, "mp", split_axis=0, concat_axis=0, tiled=True)


def hidden_kernel(features_ref, weight_ref, cotangent_ref, out_ref, pre_ref, grad_ref, held_ref):
    phase, step = pl.program_id(0), pl.program_id(1)
    steps = pl.num_programs(1)
    per_step, _, d_blk = features_ref.shape
    rows = per_step * d_blk

    @pl.when(phase == 0)
    def _():
        @pl.when(step == 0)
        def _():
            pre_ref[...] = jnp.zeros_like(pre_ref)

        held_ref[pl.ds(pl.multiple_of(step * rows, rows), rows), :] = weight_ref[...]
        acc = pre_ref[...]
        for jj in range(per_step):
            acc = acc + jnp.dot(
                features_ref[jj], weight_ref[jj * d_blk:(jj + 1) * d_blk, :],
                preferred_element_type=jnp.float32,
            )
        pre_ref[...] = acc

        @pl.when(step == steps - 1)
        def _():
            grad_ref[...] = (
                cotangent_ref[...].astype(jnp.float32) * gelu_slope(pre_ref[...])
            ).astype(grad_ref.dtype)

    @pl.when(phase == 1)
    def _():
        hidden_grad = grad_ref[...]
        for jj in range(per_step):
            start = pl.multiple_of(step * rows + jj * d_blk, d_blk)
            out_ref[jj] = lax.dot_general(
                hidden_grad, held_ref[pl.ds(start, d_blk), :],
                (((1,), (1,)), ((), ())), preferred_element_type=jnp.float32,
            ).astype(out_ref.dtype)


def block_parts_of(features, weight, cotangent, steps=2):
    n_blk, slots, d_blk = features.shape
    d_model, ff = weight.shape
    per_step = n_blk // steps
    last = steps - 1
    return pl.pallas_call(
        hidden_kernel,
        out_shape=jax.ShapeDtypeStruct((n_blk, slots, d_blk), jnp.bfloat16),
        grid=(2, steps),
        in_specs=[
            pl.BlockSpec((per_step, slots, d_blk), lambda p, j: (j * (1 - p) + last * p, 0, 0)),
            pl.BlockSpec((per_step * d_blk, ff), lambda p, j: (j * (1 - p) + last * p, 0)),
            pl.BlockSpec((slots, ff), lambda p, j: (0, 0)),
        ],
        out_specs=pl.BlockSpec((per_step, slots, d_blk), lambda p, j: (j * p, 0, 0)),
        scratch_shapes=[
            pltpu.VMEM((slots, ff), jnp.float32),
            pltpu.VMEM((slots, ff), jnp.bfloat16),
            pltpu.VMEM((d_model, ff), jnp.bfloat16),
        ],
        compiler_params=pltpu.CompilerParams(dimension_semantics=("arbitrary", "arbitrary")),
        cost_estimate=pl.CostEstimate(
            flops=4 * slots * d_model * ff,
            transcendentals=slots * ff,
            bytes_accessed=2 * (2 * features.size + weight.size + cotangent.size),
        ),
    )(features, weight, cotangent)


def reduce_scatter_mp(parts):
    arrived = lax.all_to_all(parts, "mp", split_axis=0, concat_axis=0, tiled=True)
    return jnp.sum(arrived.astype(jnp.float32), axis=0)


def per_device(tokens, expert_ids, seq_lengths, hidden_cotangent, w_in):
    tok_dev = tokens.shape[0]
    experts = w_in.shape[0] * lax.axis_size("expert")
    capacity = max(2, 2 * tok_dev // experts)
    position = jnp.arange(tok_dev, dtype=jnp.int32)
    seq_index = position // SEQ_LEN
    seq_length = jnp.sum(
        jnp.where(
            seq_index[:, None] == jnp.arange(seq_lengths.shape[0], dtype=jnp.int32)[None, :],
            seq_lengths[None, :],
            0,
        ),
        axis=1,
    )
    live_mask = position % SEQ_LEN < seq_length
    expert_row = expert_ids[:, 0]
    same_before = (
        (expert_row[None, :] == expert_row[:, None])
        & live_mask[None, :]
        & (position[None, :] < position[:, None])
    ).astype(jnp.int32)
    offset = jnp.where(position[None, :] == 0, expert_row[:, None] * capacity, 0)
    target = jnp.sum(same_before + offset, axis=1)
    slot_ids = jnp.arange(experts * capacity, dtype=jnp.int32)
    slot_hot = ((target[:, None] == slot_ids[None, :]) & live_mask[:, None]).astype(tokens.dtype)
    buffer = lax.dot_general(
        slot_hot, tokens, (((0,), (0,)), ((), ())), preferred_element_type=jnp.float32
    ).astype(tokens.dtype)
    arrived = lax.all_to_all(
        buffer.reshape((experts, capacity) + tokens.shape[1:]),
        "expert",
        split_axis=0,
        concat_axis=0,
        tiled=True,
    )
    slot_count = arrived.shape[0] * capacity
    n_mp = lax.axis_size("mp")
    blocks = gather_mp(arrived.reshape(slot_count, arrived.shape[2]))
    block_parts = block_parts_of(blocks, w_in[0], hidden_cotangent[0])
    summed = reduce_scatter_mp(block_parts).astype(jnp.bfloat16)
    returned = lax.all_to_all(
        summed.reshape(arrived.shape[0], capacity, summed.shape[1]),
        "expert",
        split_axis=0,
        concat_axis=0,
        tiled=True,
    )
    flat_rows = returned.reshape((experts * capacity,) + returned.shape[2:])
    return jnp.dot(slot_hot, flat_rows, preferred_element_type=jnp.float32).astype(flat_rows.dtype)


def solution(mesh):
    in_specs = (
        P("expert", "mp"),
        P("expert", None),
        P("expert"),
        P("expert", None, "mp"),
        P("expert", None, "mp"),
    )
    out_specs = P("expert", "mp")
    return jax.shard_map(
        per_device, mesh=mesh, in_specs=in_specs, out_specs=out_specs, check_vma=False
    )
```

```python
import math

import numpy as np

import jax
import jax.numpy as jnp
from jax import lax
from jax.experimental import pallas as pl
from jax.experimental.pallas import tpu as pltpu
from jax.sharding import PartitionSpec as P

SEQ_LEN = 128


def gelu_slope(preact):
    coeff = math.sqrt(2.0 / math.pi)
    squashed = jnp.tanh(coeff * (preact + 0.044715 * preact * preact * preact))
    return 0.5 * (1.0 + squashed) + 0.5 * preact * (1.0 - squashed * squashed) * coeff * (
        1.0 + 3.0 * 0.044715 * preact * preact
    )


def gather_mp(block):
    n_mp = lax.axis_size("mp")
    copies = jnp.broadcast_to(block[None], (n_mp,) + block.shape)
    return lax.all_to_all(copies, "mp", split_axis=0, concat_axis=0, tiled=True)


def hidden_kernel(features_ref, weight_ref, cotangent_ref, out_ref, pre_ref, grad_ref, held_ref):
    phase, step = pl.program_id(0), pl.program_id(1)
    steps = pl.num_programs(1)
    per_step, _, d_blk = features_ref.shape
    rows = per_step * d_blk

    @pl.when(phase == 0)
    def _():
        @pl.when(step == 0)
        def _():
            pre_ref[...] = jnp.zeros_like(pre_ref)

        held_ref[pl.ds(pl.multiple_of(step * rows, rows), rows), :] = weight_ref[...]
        acc = pre_ref[...]
        for jj in range(per_step):
            acc = acc + jnp.dot(
                features_ref[jj], weight_ref[jj * d_blk:(jj + 1) * d_blk, :],
                preferred_element_type=jnp.float32,
            )
        pre_ref[...] = acc

        @pl.when(step == steps - 1)
        def _():
            grad_ref[...] = (
                cotangent_ref[...].astype(jnp.float32) * gelu_slope(pre_ref[...])
            ).astype(grad_ref.dtype)

    @pl.when(phase == 1)
    def _():
        hidden_grad = grad_ref[...]
        for jj in range(per_step):
            start = pl.multiple_of(step * rows + jj * d_blk, d_blk)
            out_ref[jj] = lax.dot_general(
                hidden_grad, held_ref[pl.ds(start, d_blk), :],
                (((1,), (1,)), ((), ())), preferred_element_type=jnp.float32,
            ).astype(out_ref.dtype)


def block_parts_of(features, weight, cotangent, steps=2):
    n_blk, slots, d_blk = features.shape
    d_model, ff = weight.shape
    per_step = n_blk // steps
    last = steps - 1
    return pl.pallas_call(
        hidden_kernel,
        out_shape=jax.ShapeDtypeStruct((n_blk, slots, d_blk), jnp.bfloat16),
        grid=(2, steps),
        in_specs=[
            pl.BlockSpec((per_step, slots, d_blk), lambda p, j: (j * (1 - p) + last * p, 0, 0)),
            pl.BlockSpec((per_step * d_blk, ff), lambda p, j: (j * (1 - p) + last * p, 0)),
            pl.BlockSpec((slots, ff), lambda p, j: (0, 0)),
        ],
        out_specs=pl.BlockSpec((per_step, slots, d_blk), lambda p, j: (j * p, 0, 0)),
        scratch_shapes=[
            pltpu.VMEM((slots, ff), jnp.float32),
            pltpu.VMEM((slots, ff), jnp.bfloat16),
            pltpu.VMEM((d_model, ff), jnp.bfloat16),
        ],
        compiler_params=pltpu.CompilerParams(dimension_semantics=("arbitrary", "arbitrary")),
        cost_estimate=pl.CostEstimate(
            flops=4 * slots * d_model * ff,
            transcendentals=slots * ff,
            bytes_accessed=2 * (2 * features.size + weight.size + cotangent.size),
        ),
    )(features, weight, cotangent)


def reduce_scatter_mp(parts):
    arrived = lax.all_to_all(parts, "mp", split_axis=0, concat_axis=0, tiled=True)
    return jnp.sum(arrived.astype(jnp.float32), axis=0)


def per_device(tokens, expert_ids, seq_lengths, hidden_cotangent, w_in):
    tok_dev = tokens.shape[0]
    experts = w_in.shape[0] * lax.axis_size("expert")
    capacity = max(2, 2 * tok_dev // experts)
    position = jnp.arange(tok_dev, dtype=jnp.int32)
    seq_index = position // SEQ_LEN
    seq_length = jnp.sum(
        jnp.where(
            seq_index[:, None] == jnp.arange(seq_lengths.shape[0], dtype=jnp.int32)[None, :],
            seq_lengths[None, :],
            0,
        ),
        axis=1,
    )
    live_mask = position % SEQ_LEN < seq_length
    expert_row = expert_ids[:, 0]
    picks = (expert_row[:, None] == jnp.arange(experts, dtype=jnp.int32)[None, :]) & live_mask[:, None]
    picks = picks.astype(jnp.bfloat16)
    earlier = (position[None, :] < position[:, None]).astype(jnp.bfloat16)
    before = jnp.dot(earlier, picks, preferred_element_type=jnp.float32)
    first_slot = jnp.asarray(np.arange(experts, dtype=np.float32) * capacity)
    target = jnp.sum((before + first_slot[None, :]) * picks.astype(jnp.float32), axis=1)
    slot_ids = jnp.asarray(np.arange(experts * capacity, dtype=np.float32))
    slot_hot = ((target[:, None] == slot_ids[None, :]) & live_mask[:, None]).astype(tokens.dtype)
    buffer = lax.dot_general(
        slot_hot, tokens, (((0,), (0,)), ((), ())), preferred_element_type=jnp.float32
    ).astype(tokens.dtype)
    arrived = lax.all_to_all(
        buffer.reshape((experts, capacity) + tokens.shape[1:]),
        "expert",
        split_axis=0,
        concat_axis=0,
        tiled=True,
    )
    slot_count = arrived.shape[0] * capacity
    n_mp = lax.axis_size("mp")
    blocks = gather_mp(arrived.reshape(slot_count, arrived.shape[2]))
    block_parts = block_parts_of(blocks, w_in[0], hidden_cotangent[0])
    summed = reduce_scatter_mp(block_parts).astype(jnp.bfloat16)
    returned = lax.all_to_all(
        summed.reshape(arrived.shape[0], capacity, summed.shape[1]),
        "expert",
        split_axis=0,
        concat_axis=0,
        tiled=True,
    )
    flat_rows = returned.reshape((experts * capacity,) + returned.shape[2:])
    return jnp.dot(slot_hot, flat_rows, preferred_element_type=jnp.float32).astype(flat_rows.dtype)


def solution(mesh):
    in_specs = (
        P("expert", "mp"),
        P("expert", None),
        P("expert"),
        P("expert", None, "mp"),
        P("expert", None, "mp"),
    )
    out_specs = P("expert", "mp")
    return jax.shard_map(
        per_device, mesh=mesh, in_specs=in_specs, out_specs=out_specs, check_vma=False
    )
```
